256 devices in a mesh: tile: 32 (over x, z), sec: 8 (over y, core).
Axes of the slice: x: 4, y: 4, z: 8, core: 2. Of those that a mesh axis runs over, the one named last changes fastest.
Arguments:
- displacement: float32 [16, 2, 512, 1024], P('sec', None, 'tile'), may hold values from -0.15 to 0.15
- velocity: float32 [16, 2, 512, 1024], P('sec', None, 'tile'), may hold values from -6 to 6
- stiffness: bfloat16 [16, 4, 512, 1024], P('sec', None, 'tile'), may hold values from 0.29882812 to 3
- anchor: float32 [2, 512, 1024], P(None, 'tile'), may hold values from -0.15 to 0.15
- match_source: int32 [16, 8192], P('sec', 'tile'), may hold values from 0 to 16383
- match_target: int32 [16, 8192], P('sec', 'tile'), may hold values from 0 to 16383
- match_weight: float32 [16, 8192], P('sec', 'tile'), may hold values from 1 to 8
- match_count: int32 [16, 32], P('sec', 'tile'), may hold values from 1 to 256, 4096 in all within a row
- reset_mask: int32 [2, 16], P(None, 'sec'), may hold values 0 or 1
Outputs:
- new_displacement: float32 [16, 2, 512, 1024], P('sec', None, 'tile')
- new_velocity: float32 [16, 2, 512, 1024], P('sec', None, 'tile')
The draws below stay inside these ranges and needn't reach their ends.
Inputs may be any that keep to these rules, and one draw needn't show every extreme that they name: `match_count`: in every section the largest count is 256.
All inputs are finite; a program needn't handle non-finite values. No bound on the sum of `match_count` or of `reset_mask` on one device may be relied on, other than what follows from the above.
Results may differ from the reference program's by a relative error of at most 0.00055.
Values may be sent and summed in bfloat16 or wider, within the bound.
No kernel may reach another device: no remote copies, remote signals or barrier semaphores. Data moves between devices by JAX's collectives and lax.ppermute only.
A program may use at most 128 MiB of HBM per device.

```python
import math
import jax
import jax.numpy as jnp
import numpy as np
from jax import lax

ROWS_DEV = 16
COLS = 1024
MATCH_DEV = 256
ITERS = 2
SECTIONS = 16
ROWS = 512
SLOTS = 8192
N_TILE = 32


def draw_displacement(key, part):
    first_key = jax.random.fold_in(key, 0)
    ramp = (0.05 + 0.1 * jnp.arange(ROWS, dtype=jnp.float32) / ROWS)[:, None]
    shape = (SECTIONS, 2, ROWS, COLS)
    base = jax.random.uniform(first_key, shape, jnp.float32, -1.0, 1.0)
    return base * ramp


def draw_velocity(key, part):
    first_key = jax.random.fold_in(key, 0)
    ramp = (0.5 + jnp.arange(ROWS, dtype=jnp.float32) / ROWS)[:, None]
    shape = (SECTIONS, 2, ROWS, COLS)
    base = jax.random.truncated_normal(first_key, -3.0, 3.0, shape, jnp.float32)
    return base * ramp


def place_ends(entries, stream_key, smallest, top_value):
    longest = entries.shape.index(max(entries.shape))
    spots = []
    for shift in (0, 1):
        where = [jax.random.randint(jax.random.fold_in(stream_key, axis), (), 0, length) for axis, length in enumerate(entries.shape)]
        where[longest] = (where[longest] + shift) % entries.shape[longest]
        spots.append(tuple(where))
    return entries.at[spots[0]].set(smallest).at[spots[1]].set(top_value)


def block_levels(rng, shape, pieces, low, top_value):
    loudness = 1.0
    for dim, shards_of in pieces:
        heights = jax.random.uniform(jax.random.fold_in(jax.random.fold_in(rng, 6), dim), (shards_of,), jnp.float32, low / len(pieces), top_value / len(pieces))
        loudness = loudness * jnp.repeat(jnp.exp(heights), shape[dim] // shards_of).reshape((-1,) + (1,) * (len(shape) - 1 - dim))
    return loudness


def length_profile(count, total, most, slope):
    weights = [(1 << 20) // math.isqrt(rank ** slope) + 1 for rank in range(2, count + 1)]
    spare, holding = total - most - (count - 1), [1] * (count - 1)
    while spare > 0:
        candidates = [i for i in range(count - 1) if holding[i] < most]
        mass, remaining = sum([weights[i] for i in candidates]), spare
        for i in candidates:
            more = min(most - holding[i], max(1, remaining * weights[i] // mass), spare)
            holding[i] = holding[i] + more
            spare = spare - more
    return np.array([most] + holding)


def ragged_sizes(stream_key, count, total, bound, lean):
    if count == 2:
        one = jax.random.randint(stream_key, (), max(1, total - bound), min(bound, total - 1) + 1)
        return jnp.stack([one, total - one])
    sizes = jnp.asarray(length_profile(count, total, bound, lean), jnp.int32)
    pairs = (count - 1) // 2
    giver, taker = sizes[1:1 + 2 * pairs:2], sizes[2:2 + 2 * pairs:2]
    margin = jnp.minimum(giver - 1, bound - taker)
    shifted = jax.random.randint(jax.random.fold_in(stream_key, 1), (pairs,), 0, 1 << 20) % (margin + 1)
    sizes = sizes.at[1:1 + 2 * pairs:2].set(giver - shifted).at[2:2 + 2 * pairs:2].set(taker + shifted)
    return sizes[jax.random.permutation(jax.random.fold_in(stream_key, 2), count)]


def setup_inputs(seed: int = 0) -> dict:
    key_list = jax.random.split(jax.random.key(seed), 10)
    displacement = draw_displacement(jax.random.fold_in(key_list[9], 71), 0)
    velocity = draw_velocity(jax.random.fold_in(key_list[9], 71), 0)
    stiffness = jnp.clip(jnp.exp(math.log(3.0) - 2.306499 * jax.random.uniform(key_list[2], (SECTIONS, 4, ROWS, COLS), jnp.float32) ** block_levels(key_list[2], (SECTIONS, 4, ROWS, COLS), ((0, 8), (2, 32)), -0.2, 0.2)), 0.29882812, 3.0).astype(jnp.bfloat16)
    anchor = jnp.clip(jax.random.uniform(key_list[3], (2, ROWS, COLS), jnp.float32, -0.15, 0.15) * block_levels(key_list[3], (2, ROWS, COLS), ((1, 32),), -0.4, 0.0), -0.15, 0.15)
    match_source = place_ends(jax.random.randint(key_list[4], (SECTIONS, SLOTS), 0, ROWS_DEV * COLS), jax.random.fold_in(key_list[4], 1), 0, (ROWS_DEV * COLS) - 1).astype(jnp.int32)
    match_target = place_ends(jax.random.randint(key_list[5], (SECTIONS, SLOTS), 0, ROWS_DEV * COLS), jax.random.fold_in(key_list[5], 1), 0, (ROWS_DEV * COLS) - 1).astype(jnp.int32)
    match_weight = jnp.clip(jnp.exp(math.log(8.0) - 2.0794415 * jax.random.uniform(key_list[6], (SECTIONS, SLOTS), jnp.float32) ** block_levels(key_list[6], (SECTIONS, SLOTS), ((0, 8), (1, 32)), -0.2, 0.2)), 1.0, 8.0)
    match_count = jax.vmap(lambda own: ragged_sizes(own, N_TILE, N_TILE * MATCH_DEV // 2, MATCH_DEV, 2))(jax.random.split(key_list[7], SECTIONS)).reshape((SECTIONS, N_TILE)).astype(jnp.int32)
    reset_mask = place_ends((jax.random.randint(key_list[8], (ITERS, SECTIONS), 0, 4) < 1).astype(jnp.int32), jax.random.fold_in(key_list[8], 1), 0, 1)
    return {"displacement": displacement, "velocity": velocity, "stiffness": stiffness, "anchor": anchor, "match_source": match_source, "match_target": match_target, "match_weight": match_weight, "match_count": match_count, "reset_mask": reset_mask}


max_step = 0.05
time_step = 0.5
mixing = 0.1
epsilon = 1e-06
diagonal_rest = 1.4142135623730951

def from_left(values):
    return jnp.concatenate([jnp.zeros_like(values[..., :1]), values[..., :-1]], axis=-1)

def from_right(values):
    return jnp.concatenate([values[..., 1:], jnp.zeros_like(values[..., :1])], axis=-1)

def bond_force(first_gap, second_gap, spring_stiff, rest):
    stretch_len = jnp.sqrt(first_gap * first_gap + second_gap * second_gap)
    factor = spring_stiff * (stretch_len - rest) / stretch_len
    return (factor * first_gap, factor * second_gap)

def spring_force(padded, springs, row_start, total_rows):
    band_rows = padded.shape[-2] - 2
    columns = padded.shape[-1]
    stiff_all = springs.astype(jnp.float32)
    bond_rows = row_start - 1 + lax.iota(jnp.int32, band_rows + 1)
    row_valid = ((bond_rows >= 0) & (bond_rows + 1 < total_rows)).astype(jnp.float32)[:, None]
    column_ids = lax.iota(jnp.int32, columns)
    has_right = (column_ids < columns - 1).astype(jnp.float32)
    has_left = (column_ids >= 1).astype(jnp.float32)
    upper_first = padded[..., 0, :-1, :]
    upper_second = padded[..., 1, :-1, :]
    lower_first = padded[..., 0, 1:, :]
    lower_second = padded[..., 1, 1:, :]
    south = bond_force(1.0 + lower_first - upper_first, lower_second - upper_second, stiff_all[..., 1, :, :] * row_valid, 1.0)
    south_east = bond_force(1.0 + from_right(lower_first) - upper_first, 1.0 + from_right(lower_second) - upper_second, stiff_all[..., 2, :, :] * row_valid * has_right, diagonal_rest)
    south_west = bond_force(1.0 + from_left(lower_first) - upper_first, -1.0 + from_left(lower_second) - upper_second, stiff_all[..., 3, :, :] * row_valid * has_left, diagonal_rest)
    middle_first = padded[..., 0, 1:-1, :]
    middle_second = padded[..., 1, 1:-1, :]
    east = bond_force(from_right(middle_first) - middle_first, 1.0 + from_right(middle_second) - middle_second, stiff_all[..., 0, 1:, :] * has_right, 1.0)

    def summed(part):
        result = south[part][..., 1:, :] - south[part][..., :-1, :]
        result = result + south_east[part][..., 1:, :] - from_left(south_east[part][..., :-1, :])
        result = result + south_west[part][..., 1:, :] - from_right(south_west[part][..., :-1, :])
        return result + east[part] - from_left(east[part])
    return jnp.stack([summed(0), summed(1)], axis=-3)

def pick_nodes(values, index):
    return jax.vmap(lambda field, where: field[:, where])(values, index)

def place_nodes(target, index, amount):
    return jax.vmap(lambda field, where, extra: field.at[:, where].add(extra))(target, index, amount)

def reference(displacement, velocity, stiffness, anchor, match_source, match_target, match_weight, match_count, reset_mask):
    nodes = ROWS * COLS
    springs = jnp.concatenate([jnp.zeros((SECTIONS, 4, 1, COLS), jnp.bfloat16), stiffness], axis=2)
    slot_ids = lax.iota(jnp.int32, SLOTS)
    band_of = slot_ids // MATCH_DEV
    within = slot_ids % MATCH_DEV
    slot_live = (within[None, :] < match_count[:, band_of]).astype(jnp.float32)
    weight_live = match_weight * slot_live
    offset = (band_of * (ROWS_DEV * COLS)).astype(jnp.int32)
    source_node = match_source + offset[None, :]
    target_node = match_target + offset[None, :]
    current = displacement
    speed = velocity
    for iteration in range(ITERS):

        def section_force(pair):
            field, spring_part = pair
            padded = jnp.pad(field, ((0, 0), (1, 1), (0, 0)))
            return spring_force(padded, spring_part, 0, ROWS)
        force = lax.map(section_force, (current, springs)).reshape(SECTIONS, 2, nodes)
        flat = current.reshape(SECTIONS, 2, nodes)
        following = jnp.concatenate([flat[1:], anchor.reshape(1, 2, nodes)], axis=0)
        source_points = pick_nodes(flat, source_node)
        target_points = pick_nodes(following, target_node)
        match_force = weight_live[:, None, :] * (target_points - source_points)
        force = place_nodes(force, source_node, match_force)
        upper_part = place_nodes(force[1:], target_node[:-1], -match_force[:-1])
        force = jnp.concatenate([force[:1], upper_part], axis=0).reshape(SECTIONS, 2, ROWS, COLS)
        velocity_mid = speed + time_step * force
        force_sq = lax.optimization_barrier(jnp.sum(force * force, axis=(1, 2, 3)))
        speed_sq = lax.optimization_barrier(jnp.sum(velocity_mid * velocity_mid, axis=(1, 2, 3)))
        speed_ratio = jnp.sqrt(speed_sq) / jnp.sqrt(force_sq + epsilon)
        speed = (1.0 - mixing) * velocity_mid + mixing * speed_ratio[:, None, None, None] * force
        keep = (1 - reset_mask[iteration]).astype(jnp.float32)
        speed = speed * keep[:, None, None, None]
        current = current + max_step * jnp.tanh(time_step * speed / max_step)
    return (current, speed)
```

```python
import jax
import jax.numpy as jnp
from jax import lax
from jax.experimental import pallas as pl
from jax.experimental.pallas import tpu as pltpu
from jax.sharding import PartitionSpec as P

ITERS = 2


max_step = 0.05
time_step = 0.5
mixing = 0.1
epsilon = 1e-06
diagonal_rest = 1.4142135623730951
HIGHEST = lax.Precision.HIGHEST


def shifted(value, axis, steps):
    count = lax.axis_size(axis)
    pairs = [(i, i + steps) for i in range(count) if 0 <= i + steps < count]
    return lax.ppermute(value, axis, pairs)


def tile_sum(value):
    count = lax.axis_size("tile")
    if count & (count - 1):
        return lax.psum(value, "tile")
    step = 1
    while step < count:
        value = value + lax.ppermute(value, "tile", [(i, i ^ step) for i in range(count)])
        step *= 2
    return value


def bond(first_gap, second_gap, spring_stiff, rest):
    stretch_len = jnp.sqrt(first_gap * first_gap + second_gap * second_gap)
    factor = spring_stiff * (stretch_len - rest) / stretch_len
    return (factor * first_gap, factor * second_gap)


def spring_kernel(u_ref, top_ref, bot_ref, k_ref, kt_ref, keep_ref, out_ref):
    sections, _, rows, columns = u_ref.shape
    row = lax.broadcasted_iota(jnp.int32, (rows, columns), 0)
    col = lax.broadcasted_iota(jnp.int32, (rows, columns), 1)
    col_one = lax.broadcasted_iota(jnp.int32, (1, columns), 1)
    keep_top = keep_ref[0:1, :]
    keep_bot = keep_ref[1:2, :]
    last_row = row == rows - 1
    down_keep = jnp.where(last_row, keep_bot, 1.0)

    def east_of(x):
        return pltpu.roll(x, columns - 1, 1)

    def west_of(x):
        return pltpu.roll(x, 1, 1)

    for s in range(sections):
        x0 = u_ref[s, 0]
        x1 = u_ref[s, 1]
        t0 = top_ref[s, 0]
        t1 = top_ref[s, 1]
        l0 = jnp.where(last_row, bot_ref[s, 0], pltpu.roll(x0, rows - 1, 0))
        l1 = jnp.where(last_row, bot_ref[s, 1], pltpu.roll(x1, rows - 1, 0))
        k_east = jnp.where(col < columns - 1, k_ref[s, 0].astype(jnp.float32), 0.0)
        k_south = k_ref[s, 1].astype(jnp.float32) * down_keep
        k_se = jnp.where(col < columns - 1, k_ref[s, 2].astype(jnp.float32) * down_keep, 0.0)
        k_sw = jnp.where(col >= 1, k_ref[s, 3].astype(jnp.float32) * down_keep, 0.0)
        south = bond(1.0 + l0 - x0, l1 - x1, k_south, 1.0)
        south_east = bond(
            1.0 + east_of(l0) - x0, 1.0 + east_of(l1) - x1, k_se, diagonal_rest
        )
        south_west = bond(
            1.0 + west_of(l0) - x0, -1.0 + west_of(l1) - x1, k_sw, diagonal_rest
        )
        east = bond(east_of(x0) - x0, 1.0 + east_of(x1) - x1, k_east, 1.0)
        r0 = x0[0:1, :]
        r1 = x1[0:1, :]
        kt_south = kt_ref[s, 0].astype(jnp.float32) * keep_top
        kt_se = jnp.where(col_one < columns - 1, kt_ref[s, 1].astype(jnp.float32) * keep_top, 0.0)
        kt_sw = jnp.where(col_one >= 1, kt_ref[s, 2].astype(jnp.float32) * keep_top, 0.0)
        top_south = bond(1.0 + r0 - t0, r1 - t1, kt_south, 1.0)
        top_se = bond(1.0 + east_of(r0) - t0, 1.0 + east_of(r1) - t1, kt_se, diagonal_rest)
        top_sw = bond(1.0 + west_of(r0) - t0, -1.0 + west_of(r1) - t1, kt_sw, diagonal_rest)
        for part in range(2):
            below = south[part] + west_of(south_east[part]) + east_of(south_west[part])
            below_top = top_south[part] + west_of(top_se[part]) + east_of(top_sw[part])
            incoming = jnp.where(row == 0, below_top, pltpu.roll(below, 1, 0))
            owned = south[part] + south_east[part] + south_west[part] + east[part]
            out_ref[s, part] = owned - incoming - west_of(east[part])


def spring_force(current, top, bottom, stiffness, top_stiff, keep):
    return pl.pallas_call(
        spring_kernel,
        out_shape=jax.ShapeDtypeStruct(current.shape, jnp.float32),
    )(current, top, bottom, stiffness, top_stiff, keep)


def one_hots(index, band_rows, columns):
    row = index // columns
    col = index % columns
    col_hot = (col[..., None] == lax.iota(jnp.int32, columns)).astype(jnp.float32)
    row_hot = (row[..., :, None] == lax.iota(jnp.int32, band_rows)).astype(jnp.float32)
    return col_hot, jnp.swapaxes(row_hot, -1, -2)


def gather_points(field, col_hot, row_hot):
    picked = jnp.einsum("scrk,sjk->scrj", field, col_hot, precision=HIGHEST)
    return jnp.sum(picked * row_hot[:, None], axis=2)


def scatter_points(values, col_hot, row_hot):
    spread = values[:, :, None, :] * row_hot[:, None]
    return jnp.einsum("scrj,sjk->scrk", spread, col_hot, precision=HIGHEST)


def local(
    displacement,
    velocity,
    stiffness,
    anchor,
    match_source,
    match_target,
    match_weight,
    match_count,
    reset_mask,
):
    sections, _, band_rows, columns = displacement.shape
    slots = match_source.shape[1]
    band_index = lax.axis_index("tile")
    band_total = lax.axis_size("tile")
    last_group = lax.axis_index("sec") == lax.axis_size("sec") - 1
    top_stiff = shifted(stiffness[:, 1:, band_rows - 1 :, :], "tile", 1)
    keep = jnp.stack(
        [
            jnp.where(band_index > 0, 1.0, 0.0),
            jnp.where(band_index < band_total - 1, 1.0, 0.0),
        ]
        + [jnp.float32(0.0)] * 6
    ).astype(jnp.float32)
    keep = jnp.broadcast_to(keep[:, None], (8, columns))
    slot_live = (lax.iota(jnp.int32, slots)[None, :] < match_count).astype(jnp.float32)
    weight_live = match_weight * slot_live
    target_prev = shifted(match_target[-1], "sec", 1)
    weight_prev = shifted(weight_live[-1], "sec", 1)
    gather_index = jnp.stack(
        [
            jnp.concatenate([match_source[0], target_prev]),
            jnp.concatenate([match_source[1], match_target[0]]),
        ]
    )
    col_hot, row_hot = one_hots(gather_index, band_rows, columns)
    anchor_hot = one_hots(match_target[-1:], band_rows, columns)
    anchor_points = gather_points(anchor[None], *anchor_hot)[0]
    current = displacement
    speed = velocity
    for iteration in range(ITERS):
        top = shifted(current[:, :, band_rows - 1 :, :], "tile", 1)
        bottom = shifted(current[:, :, :1, :], "tile", -1)
        points = gather_points(current, col_hot, row_hot)
        source_first = points[0, :, :slots]
        target_back = points[0, :, slots:]
        source_last = points[1, :, :slots]
        target_first = points[1, :, slots:]
        source_prev = shifted(source_last, "sec", 1)
        target_last = shifted(target_back, "sec", -1)
        target_last = jnp.where(last_group, anchor_points, target_last)
        force_first = weight_live[0] * (target_first - source_first)
        force_last = weight_live[1] * (target_last - source_last)
        force_prev = weight_prev * (target_back - source_prev)
        values = jnp.stack(
            [
                jnp.concatenate([force_first, -force_prev], axis=-1),
                jnp.concatenate([force_last, -force_first], axis=-1),
            ]
        )
        matched = scatter_points(values, col_hot, row_hot)
        force = spring_force(current, top, bottom, stiffness, top_stiff, keep) + matched
        velocity_mid = speed + time_step * force
        sums = tile_sum(
            jnp.stack(
                [
                    jnp.sum(force * force, axis=(1, 2, 3)),
                    jnp.sum(velocity_mid * velocity_mid, axis=(1, 2, 3)),
                ]
            )
        )
        force_sq, speed_sq = sums[0], sums[1]
        speed_ratio = jnp.sqrt(speed_sq) / jnp.sqrt(force_sq + epsilon)
        speed = (1.0 - mixing) * velocity_mid + mixing * speed_ratio[:, None, None, None] * force
        keep_speed = (1 - reset_mask[iteration]).astype(jnp.float32)
        speed = speed * keep_speed[:, None, None, None]
        current = current + max_step * jnp.tanh(time_step * speed / max_step)
    return (current, speed)


def solution(mesh):
    placed = (
        P("sec", None, "tile", None),
        P("sec", None, "tile", None),
        P("sec", None, "tile", None),
        P(None, "tile", None),
        P("sec", "tile"),
        P("sec", "tile"),
        P("sec", "tile"),
        P("sec", "tile"),
        P(None, "sec"),
    )
    return jax.shard_map(
        local,
        mesh=mesh,
        in_specs=placed,
        out_specs=(P("sec", None, "tile", None), P("sec", None, "tile", None)),
        check_vma=False,
    )
```

```python
import jax
import jax.numpy as jnp
from jax import lax
from jax.experimental import pallas as pl
from jax.experimental.pallas import tpu as pltpu
from jax.sharding import PartitionSpec as P

ITERS = 2


max_step = 0.05
time_step = 0.5
mixing = 0.1
epsilon = 1e-06
diagonal_rest = 1.4142135623730951
HIGHEST = lax.Precision.HIGHEST


def shifted(value, axis, steps):
    count = lax.axis_size(axis)
    pairs = [(i, i + steps) for i in range(count) if 0 <= i + steps < count]
    return lax.ppermute(value, axis, pairs)


def tile_sum(value):
    count = lax.axis_size("tile")
    if count & (count - 1):
        return lax.psum(value, "tile")
    step = 1
    while step < count:
        value = value + lax.ppermute(value, "tile", [(i, i ^ step) for i in range(count)])
        step *= 2
    return value


def bond(first_gap, second_gap, spring_stiff, rest):
    stretch_len = jnp.sqrt(first_gap * first_gap + second_gap * second_gap)
    factor = spring_stiff * (stretch_len - rest) / stretch_len
    return (factor * first_gap, factor * second_gap)


def spring_kernel(u_ref, top_ref, bot_ref, k_ref, keep_ref, out_ref):
    sections, _, rows, columns = u_ref.shape
    row = lax.broadcasted_iota(jnp.int32, (rows, columns), 0)
    col = lax.broadcasted_iota(jnp.int32, (rows, columns), 1)
    col_one = lax.broadcasted_iota(jnp.int32, (1, columns), 1)
    keep_top = keep_ref[0:1, :]
    keep_bot = keep_ref[1:2, :]
    last_row = row == rows - 1
    down_keep = jnp.where(last_row, keep_bot, 1.0)

    def east_of(x):
        return pltpu.roll(x, columns - 1, 1)

    def west_of(x):
        return pltpu.roll(x, 1, 1)

    for s in range(sections):
        x0 = u_ref[s, 0]
        x1 = u_ref[s, 1]
        t0 = top_ref[s, 0]
        t1 = top_ref[s, 1]
        l0 = jnp.where(last_row, bot_ref[s, 0], pltpu.roll(x0, rows - 1, 0))
        l1 = jnp.where(last_row, bot_ref[s, 1], pltpu.roll(x1, rows - 1, 0))
        k_east = jnp.where(col < columns - 1, k_ref[s, 0].astype(jnp.float32), 0.0)
        k_south = k_ref[s, 1].astype(jnp.float32) * down_keep
        k_se = jnp.where(col < columns - 1, k_ref[s, 2].astype(jnp.float32) * down_keep, 0.0)
        k_sw = jnp.where(col >= 1, k_ref[s, 3].astype(jnp.float32) * down_keep, 0.0)
        south = bond(1.0 + l0 - x0, l1 - x1, k_south, 1.0)
        south_east = bond(
            1.0 + east_of(l0) - x0, 1.0 + east_of(l1) - x1, k_se, diagonal_rest
        )
        south_west = bond(
            1.0 + west_of(l0) - x0, -1.0 + west_of(l1) - x1, k_sw, diagonal_rest
        )
        east = bond(east_of(x0) - x0, 1.0 + east_of(x1) - x1, k_east, 1.0)
        r0 = x0[0:1, :]
        r1 = x1[0:1, :]
        kt_south = top_ref[s, 2] * keep_top
        kt_se = jnp.where(col_one < columns - 1, top_ref[s, 3] * keep_top, 0.0)
        kt_sw = jnp.where(col_one >= 1, top_ref[s, 4] * keep_top, 0.0)
        top_south = bond(1.0 + r0 - t0, r1 - t1, kt_south, 1.0)
        top_se = bond(1.0 + east_of(r0) - t0, 1.0 + east_of(r1) - t1, kt_se, diagonal_rest)
        top_sw = bond(1.0 + west_of(r0) - t0, -1.0 + west_of(r1) - t1, kt_sw, diagonal_rest)
        for part in range(2):
            below = south[part] + west_of(south_east[part]) + east_of(south_west[part])
            below_top = top_south[part] + west_of(top_se[part]) + east_of(top_sw[part])
            incoming = jnp.where(row == 0, below_top, pltpu.roll(below, 1, 0))
            owned = south[part] + south_east[part] + south_west[part] + east[part]
            out_ref[s, part] = owned - incoming - west_of(east[part])


def spring_force(current, top, bottom, stiffness, keep):
    return pl.pallas_call(
        spring_kernel,
        out_shape=jax.ShapeDtypeStruct(current.shape, jnp.float32),
    )(current, top, bottom, stiffness, keep)


def one_hots(index, band_rows, columns):
    row = index // columns
    col = index % columns
    col_hot = (col[:, None] == lax.iota(jnp.int32, columns)[None, :]).astype(jnp.float32)
    row_hot = (lax.iota(jnp.int32, band_rows)[:, None] == row[None, :]).astype(jnp.float32)
    return col_hot, row_hot


def gather_points(field, hots):
    col_hot, row_hot = hots
    picked = jnp.einsum("crk,jk->crj", field, col_hot, precision=HIGHEST)
    return jnp.sum(picked * row_hot[None], axis=1)


def scatter_points(values, hots):
    col_hot, row_hot = hots
    spread = values[:, None, :] * row_hot[None]
    return jnp.einsum("crj,jk->crk", spread, col_hot, precision=HIGHEST)


def advanced(current, velocity_mid, force, speed_ratio, keep_speed):
    speed = (1.0 - mixing) * velocity_mid + mixing * speed_ratio * force
    speed = speed * keep_speed
    return current + max_step * jnp.tanh(time_step * speed / max_step), speed


def local(
    displacement,
    velocity,
    stiffness,
    anchor,
    match_source,
    match_target,
    match_weight,
    match_count,
    reset_mask,
):
    sections, _, band_rows, columns = displacement.shape
    slots = match_source.shape[1]
    band_index = lax.axis_index("tile")
    band_total = lax.axis_size("tile")
    last_group = lax.axis_index("sec") == lax.axis_size("sec") - 1
    keep = jnp.stack(
        [
            jnp.where(band_index > 0, 1.0, 0.0),
            jnp.where(band_index < band_total - 1, 1.0, 0.0),
        ]
        + [jnp.float32(0.0)] * 6
    ).astype(jnp.float32)
    keep = jnp.broadcast_to(keep[:, None], (8, columns))
    slot_live = (lax.iota(jnp.int32, slots)[None, :] < match_count).astype(jnp.float32)
    weight_live = match_weight * slot_live
    hots_last = one_hots(jnp.concatenate([match_source[1], match_target[0]]), band_rows, columns)
    points_last = gather_points(displacement[1], hots_last)
    forward = shifted(
        jnp.concatenate(
            [
                points_last[:, :slots],
                match_target[1][None].astype(jnp.float32),
                weight_live[1][None],
            ]
        ),
        "sec",
        1,
    )
    source_prev = forward[:2]
    target_prev = forward[2].astype(jnp.int32)
    weight_prev = forward[3]
    hots_first = one_hots(jnp.concatenate([match_source[0], target_prev]), band_rows, columns)
    points_first = gather_points(displacement[0], hots_first)
    anchor_points = gather_points(anchor, one_hots(match_target[1], band_rows, columns))
    top_stiff = stiffness[:, 1:, band_rows - 1 :, :].astype(jnp.float32)
    first_top = shifted(
        jnp.concatenate([displacement[:, :, band_rows - 1 :, :], top_stiff], axis=1), "tile", 1
    )
    top_stiff = first_top[:, 2:]
    top = first_top[:, :2]
    bottom = shifted(displacement[:, :, :1, :], "tile", -1)
    current = displacement
    speed = velocity
    for iteration in range(ITERS):
        source_first = points_first[:, :slots]
        target_back = points_first[:, slots:]
        source_last = points_last[:, :slots]
        target_first = points_last[:, slots:]
        if iteration > 0:
            source_prev = shifted(source_last, "sec", 1)
        target_last = shifted(target_back, "sec", -1)
        target_last = jnp.where(last_group, anchor_points, target_last)
        spring = spring_force(
            current, jnp.concatenate([top, top_stiff], axis=1), bottom, stiffness, keep
        )
        force_first = weight_live[0] * (target_first - source_first)
        force_last = weight_live[1] * (target_last - source_last)
        force_prev = weight_prev * (target_back - source_prev)
        matched = jnp.stack(
            [
                scatter_points(jnp.concatenate([force_first, -force_prev], axis=-1), hots_first),
                scatter_points(jnp.concatenate([force_last, -force_first], axis=-1), hots_last),
            ]
        )
        force = spring + matched
        velocity_mid = speed + time_step * force
        local_sums = jnp.stack(
            [
                jnp.sum(force * force, axis=(1, 2, 3)),
                jnp.sum(velocity_mid * velocity_mid, axis=(1, 2, 3)),
            ]
        )
        if iteration + 1 < ITERS:
            parts = jnp.concatenate([current, velocity_mid, force], axis=1)
            parts_first = gather_points(parts[0], hots_first)
            parts_last = gather_points(parts[1], hots_last)
            top_parts = shifted(parts[:, :, band_rows - 1 :, :], "tile", 1)
            bottom_parts = shifted(parts[:, :, :1, :], "tile", -1)
        sums = tile_sum(local_sums)
        force_sq, speed_sq = sums[0], sums[1]
        speed_ratio = jnp.sqrt(speed_sq) / jnp.sqrt(force_sq + epsilon)
        keep_speed = (1 - reset_mask[iteration]).astype(jnp.float32)
        ratio4 = speed_ratio[:, None, None, None]
        keep4 = keep_speed[:, None, None, None]
        current, speed = advanced(current, velocity_mid, force, ratio4, keep4)
        if iteration + 1 < ITERS:

            def moved(stacked, ratio, keep_one):
                return advanced(stacked[:2], stacked[2:4], stacked[4:], ratio, keep_one)[0]

            points_first = moved(parts_first, speed_ratio[0], keep_speed[0])
            points_last = moved(parts_last, speed_ratio[1], keep_speed[1])
            top = moved(jnp.swapaxes(top_parts, 0, 1), ratio4[:, 0], keep4[:, 0])
            top = jnp.swapaxes(top, 0, 1)
            bottom = moved(jnp.swapaxes(bottom_parts, 0, 1), ratio4[:, 0], keep4[:, 0])
            bottom = jnp.swapaxes(bottom, 0, 1)
    return (current, speed)


def solution(mesh):
    placed = (
        P("sec", None, "tile", None),
        P("sec", None, "tile", None),
        P("sec", None, "tile", None),
        P(None, "tile", None),
        P("sec", "tile"),
        P("sec", "tile"),
        P("sec", "tile"),
        P("sec", "tile"),
        P(None, "sec"),
    )
    return jax.shard_map(
        local,
        mesh=mesh,
        in_specs=placed,
        out_specs=(P("sec", None, "tile", None), P("sec", None, "tile", None)),
        check_vma=False,
    )
```
